512 devices in a mesh: sp: 128 (over z, x, y_hi, core), hd: 4 (over y_lo).
Axes of the slice: x: 4, y: 8 (y_hi: 2, y_lo: 4; y = y_hi * 4 + y_lo), z: 8, core: 2. Of those that a mesh axis runs over, the one named last changes fastest.
Arguments:
- query: bfloat16 [128, 3, 128, 2560], P('sp', None, None, 'hd'), may hold values from -8 to 8
- keys: bfloat16 [128, 3, 128, 2560], P('sp', None, None, 'hd'), may hold values from -8 to 8
- values: bfloat16 [128, 3, 128, 2560], P('sp', None, None, 'hd'), may hold values from -6 to 6
- cache_keys: bfloat16 [128, 8, 128, 2560], P('sp', None, None, 'hd'), may hold values from -6 to 6
- cache_values: bfloat16 [128, 8, 128, 2560], P('sp', None, None, 'hd'), may hold values from -6 to 6
- q_gain: float32 [2560], P('hd'), may hold values from 0.1 to 1.9
- k_gain: float32 [2560], P('hd'), may hold values from 0.1 to 1.9
- window_margins: int32 [128, 4], P('sp'), may hold values from 0 to 4
- cache_frames: int32 [128, 9, 2], replicated, may hold values from -1 to 7, as said below
Outputs:
- attn_out: bfloat16 [128, 3, 128, 2560], P('sp', None, None, 'hd')
The draws below stay inside these ranges and needn't reach their ends.
Inputs may be any that keep to these rules, and one draw needn't show every extreme that they name: cache_frames[t, d, c] is a cached frame or -1 for an empty slot; it is -1 wherever the neighbour tile t + dh * 8 + dw lies outside the grid; the frames listed for one t and d differ.
All inputs are finite; a program needn't handle non-finite values.
Results may differ from the reference program's by a relative error of at most 0.012.
Values may be sent and summed in bfloat16 or wider, within the bound.
No kernel may reach another device: no remote copies, remote signals or barrier semaphores. Data moves between devices by JAX's collectives and lax.ppermute only.
A program may use at most 64 MiB of HBM per device.

```python
import jax
import jax.numpy as jnp
from jax import lax

HS = 128
HEADS = 20
F = 3
CF = 8
TH = 8
TW = 16
GW = 8
HALO = 4
CAP = 2
TILES = 128


def query_and_keys(key):
    shape = (TILES, F, TH * TW, HEADS * HS)
    base = jax.random.fold_in(key, 17)
    parts = jax.random.split(base, 4)
    channel_head = jnp.arange(HEADS * HS, dtype=jnp.int32) // HS
    head_scale = 0.5 * 3.0 ** (channel_head.astype(jnp.float32) / max(HEADS - 1, 1))
    rough_q = jax.random.uniform(parts[0], shape, jnp.float32, 0.75, 1.25)
    rough_k = jax.random.uniform(parts[1], shape, jnp.float32, 0.75, 1.25)
    query = jnp.clip(jax.random.normal(parts[2], shape, jnp.float32), -4.0, 4.0) * head_scale * rough_q
    keys = jnp.clip(jax.random.normal(parts[3], shape, jnp.float32), -4.0, 4.0) * head_scale * rough_k
    return (query, keys)


def draw_query(key, part):
    return query_and_keys(key)[0].astype(jnp.bfloat16)


def draw_keys(key, part):
    return query_and_keys(key)[1].astype(jnp.bfloat16)


def draw_cache_frames(key, part):
    base = jax.random.fold_in(key, 29)
    first, second = jax.random.split(base, 2)
    ranking = jax.random.randint(first, (TILES, 9, CF), 0, 1 << 20) * CF + jnp.arange(CF, dtype=jnp.int32)
    ordering = jnp.argsort(ranking, axis=-1, stable=True).astype(jnp.int32)
    frames = ordering[:, :, :CAP]
    keeping = jax.random.randint(second, (TILES, 9, CAP), 0, 4) != 0
    tiles = jnp.arange(TILES, dtype=jnp.int32)
    tile_row = tiles // GW
    tile_col = tiles % GW
    slot_ids = jnp.arange(9, dtype=jnp.int32)
    row_steps = slot_ids // 3 - 1
    col_steps = slot_ids % 3 - 1
    near_row = tile_row[:, None] + row_steps[None, :]
    near_col = tile_col[:, None] + col_steps[None, :]
    inside = (near_row >= 0) & (near_row < TILES // GW) & (near_col >= 0) & (near_col < GW)
    return jnp.where(keeping & inside[:, :, None], frames, -1).astype(jnp.int32)


def touch_ends(drawn, stream_key, least, high):
    longest = drawn.shape.index(max(drawn.shape))
    spots = []
    for shift in (0, 1):
        where = [jax.random.randint(jax.random.fold_in(stream_key, axis), (), 0, length) for axis, length in enumerate(drawn.shape)]
        where[longest] = (where[longest] + shift) % drawn.shape[longest]
        spots.append(tuple(where))
    return drawn.at[spots[0]].set(least).at[spots[1]].set(high)


def block_levels(key, shape, cuts, least, high):
    def one(dim, shards_of):
        draws = jax.random.uniform(jax.random.fold_in(jax.random.fold_in(key, 6), dim), (shards_of,), jnp.float32, least / len(cuts), high / len(cuts))
        return jnp.repeat(jnp.exp(draws), shape[dim] // shards_of).reshape((-1,) + (1,) * (len(shape) - dim - 1))

    level = one(*cuts[0])
    for cut in cuts[1:]:
        level = level * one(*cut)
    return level


def noise(key, shape, scale, bound, shards=(), kind=jnp.bfloat16):
    result = scale * jax.random.normal(key, shape, jnp.float32)
    if shards:
        result = result * block_levels(key, shape, shards, -0.22, 0.18)
    return jnp.clip(result, -bound, bound).astype(kind)


def setup_inputs(seed: int = 0) -> dict:
    key_of = jax.random.split(jax.random.key(seed), 10)
    return {
        "query": draw_query(jax.random.fold_in(key_of[9], 71), 0),
        "keys": draw_keys(jax.random.fold_in(key_of[9], 71), 0),
        "values": noise(key_of[2], (TILES, F, TH * TW, HEADS * HS), 1.0, 6.0, ((0, 128), (3, 4))),
        "cache_keys": noise(key_of[3], (TILES, CF, TH * TW, HEADS * HS), 1.0, 6.0, ((0, 128), (3, 4))),
        "cache_values": noise(key_of[4], (TILES, CF, TH * TW, HEADS * HS), 1.0, 6.0, ((0, 128), (3, 4))),
        "q_gain": jnp.clip(1.0 + 0.18 * jax.random.normal(key_of[5], (HEADS * HS,), jnp.float32), 0.1, 1.9),
        "k_gain": jnp.clip(1.0 + 0.18 * jax.random.normal(key_of[6], (HEADS * HS,), jnp.float32), 0.1, 1.9),
        "window_margins": touch_ends(jax.random.randint(key_of[7], (TILES, 4), 0, HALO + 1), jax.random.fold_in(key_of[7], 1), 0, HALO).astype(jnp.int32),
        "cache_frames": draw_cache_frames(jax.random.fold_in(key_of[9], 71), 0),
    }


EPSILON = 1e-06
MASKED = -1e+30

def normalize(tensor, gain):
    wide = tensor.astype(jnp.float32)
    mean_sq = lax.optimization_barrier(jnp.mean(wide * wide, axis=-1, keepdims=True))
    return (wide * lax.rsqrt(mean_sq + EPSILON) * gain).astype(jnp.bfloat16)

def reference(query, keys, values, cache_keys, cache_values, q_gain, k_gain, window_margins, cache_frames):
    width_all = HEADS * HS
    query_normed = normalize(query, q_gain)
    keys_normed = normalize(keys, k_gain)
    grid_rows = TILES // GW

    def to_grid(tensor):
        shaped = tensor.reshape(grid_rows, GW, F, TH, TW, width_all)
        return jnp.transpose(shaped, (2, 0, 3, 1, 4, 5)).reshape(F, grid_rows * TH, GW * TW, width_all)
    padding = ((0, 0), (HALO, HALO), (HALO, HALO), (0, 0))
    key_pad = jnp.pad(to_grid(keys_normed), padding)
    value_pad = jnp.pad(to_grid(values), padding)
    slot_ids = jnp.arange(9, dtype=jnp.int32)
    row_steps = slot_ids // 3 - 1
    col_steps = slot_ids % 3 - 1
    score_scale = HS ** (-0.5)

    def one_tile(tile):
        tile_row = tile // GW
        tile_col = tile % GW
        zero_index = jnp.zeros((), jnp.int32)
        corner = (zero_index, tile_row * TH, tile_col * TW, zero_index)
        extent = (F, TH + 2 * HALO, TW + 2 * HALO, width_all)
        window_k = lax.dynamic_slice(key_pad, corner, extent).reshape(-1, width_all)
        window_v = lax.dynamic_slice(value_pad, corner, extent).reshape(-1, width_all)
        margins = window_margins[tile]
        row_pos = jnp.arange(TH + 2 * HALO, dtype=jnp.int32)
        row_global = tile_row * TH - HALO + row_pos
        row_valid = (row_global >= 0) & (row_global < grid_rows * TH) & (row_pos >= HALO - margins[0]) & (row_pos < HALO + TH + margins[1])
        col_pos = jnp.arange(TW + 2 * HALO, dtype=jnp.int32)
        col_global = tile_col * TW - HALO + col_pos
        col_valid = (col_global >= 0) & (col_global < GW * TW) & (col_pos >= HALO - margins[2]) & (col_pos < HALO + TW + margins[3])
        window_valid = jnp.broadcast_to((row_valid[:, None] & col_valid[None, :])[None], (F, TH + 2 * HALO, TW + 2 * HALO)).reshape(-1)
        neighbour = jnp.clip(tile + row_steps * GW + col_steps, 0, TILES - 1).astype(jnp.int32)
        listed = cache_frames[tile]
        wanted = jnp.maximum(listed, 0).astype(jnp.int32)
        cached_k = cache_keys[neighbour[:, None], wanted].reshape(-1, width_all)
        cached_v = cache_values[neighbour[:, None], wanted].reshape(-1, width_all)
        cache_valid = jnp.broadcast_to((listed >= 0)[:, :, None], (9, CAP, TH * TW)).reshape(-1)
        all_keys = jnp.concatenate([window_k, cached_k], axis=0).reshape(-1, HEADS, HS)
        all_values = jnp.concatenate([window_v, cached_v], axis=0).reshape(-1, HEADS, HS)
        all_valid = jnp.concatenate([window_valid, cache_valid], axis=0)
        tile_query = query_normed[tile].reshape(F * TH * TW, HEADS, HS)
        scores = jnp.einsum('qhc,khc->hqk', tile_query.astype(jnp.float32), all_keys.astype(jnp.float32)) * score_scale
        scores = jnp.where(all_valid[None, None, :], scores, MASKED)
        row_top = lax.optimization_barrier(jnp.max(scores, axis=-1, keepdims=True))
        expo = jnp.exp(scores - row_top)
        probs = (expo / lax.optimization_barrier(jnp.sum(expo, axis=-1, keepdims=True))).astype(jnp.bfloat16)
        mixed_out = jnp.einsum('hqk,khc->qhc', probs.astype(jnp.float32), all_values.astype(jnp.float32))
        return mixed_out.astype(jnp.bfloat16).reshape(F, TH * TW, width_all)
    return lax.map(one_tile, jnp.arange(TILES, dtype=jnp.int32))
```

```python
import jax
import jax.numpy as jnp
from jax import lax
from jax.sharding import PartitionSpec as P
from jax.experimental import pallas as pl
from jax.experimental.pallas import tpu as pltpu

HS = 128
TH = 8
TW = 16
GW = 8
HALO = 4


EPSILON = 1e-06
MASKED = -1e30


def shifted(x, axis, by):
    size = lax.axis_size(axis)
    pairs = [(i, i + by) for i in range(size) if 0 <= i + by < size]
    return lax.ppermute(x, axis, pairs)


def edge_part(grid, row_step, col_step):
    if row_step == -1:
        grid = grid[:, TH - HALO :]
    elif row_step == 1:
        grid = grid[:, :HALO]
    if col_step == -1:
        grid = grid[:, :, TW - HALO :]
    elif col_step == 1:
        grid = grid[:, :, :HALO]
    return grid


def slot_of(row_step, col_step):
    return 3 * (row_step + 1) + (col_step + 1)


def normalize(tensor, gain, row_total, width_all):
    wide = tensor.astype(jnp.float32)
    factor = lax.rsqrt(row_total / width_all + EPSILON)
    return (wide * factor[..., None] * gain).astype(jnp.bfloat16)


def attend_kernel(wvalid_ref, cvalid_ref, q_ref, wk_ref, ck_ref, wv_ref, cv_ref, o_ref):
    score_scale = HS ** (-0.5)
    dims = (((1,), (1,)), ((), ()))
    head_q = q_ref[...]
    window_scores = (
        lax.dot_general(head_q, wk_ref[...], dims, preferred_element_type=jnp.float32)
        * score_scale
    )
    window_scores = jnp.where(wvalid_ref[...] > 0, window_scores, MASKED)
    cache_scores = (
        lax.dot_general(head_q, ck_ref[...], dims, preferred_element_type=jnp.float32)
        * score_scale
    )
    cache_scores = jnp.where(cvalid_ref[...] > 0, cache_scores, MASKED)
    row_top = jnp.maximum(
        jnp.max(window_scores, axis=1, keepdims=True), jnp.max(cache_scores, axis=1, keepdims=True)
    )
    window_exp = jnp.exp(window_scores - row_top)
    cache_exp = jnp.exp(cache_scores - row_top)
    row_total = jnp.sum(window_exp, axis=1, keepdims=True) + jnp.sum(
        cache_exp, axis=1, keepdims=True
    )
    window_probs = (window_exp / row_total).astype(jnp.bfloat16)
    cache_probs = (cache_exp / row_total).astype(jnp.bfloat16)
    mixed_out = jnp.dot(window_probs, wv_ref[...], preferred_element_type=jnp.float32) + jnp.dot(
        cache_probs, cv_ref[...], preferred_element_type=jnp.float32
    )
    o_ref[...] = mixed_out.astype(jnp.bfloat16)


def body(
    query, keys, values, cache_keys, cache_values, q_gain, k_gain, window_margins, cache_frames
):
    frames_now = query.shape[1]
    tile_len = query.shape[2]
    channels = query.shape[3]
    width_all = channels * lax.axis_size("hd")
    query_wide = query[0].astype(jnp.float32)
    keys_wide = keys[0].astype(jnp.float32)
    query_total, keys_total = lax.psum(
        (jnp.sum(query_wide * query_wide, axis=-1), jnp.sum(keys_wide * keys_wide, axis=-1)), "hd"
    )
    query_normed = normalize(query[0], q_gain, query_total, width_all)
    keys_normed = normalize(keys[0], k_gain, keys_total, width_all)
    key_grid = keys_normed.reshape(frames_now, TH, TW, channels)
    value_grid = values[0].reshape(frames_now, TH, TW, channels)
    own_place = lax.axis_index("sp")
    tile_count = lax.axis_size("sp")
    grid_rows = tile_count // GW
    own_cache_k = cache_keys[0]
    own_cache_v = cache_values[0]

    def blocks_for(target, slot_index):
        safe_target = jnp.clip(target, 0, tile_count - 1)
        listed = lax.dynamic_index_in_dim(cache_frames, safe_target, 0, keepdims=False)[slot_index]
        wanted = jnp.maximum(listed, 0)
        return (own_cache_k[wanted], own_cache_v[wanted])

    center_k, center_v = blocks_for(own_place, 4)
    arrived = {}
    for row_step in (-1, 0, 1):
        for col_step in (-1, 0, 1):
            if not (row_step == 0 and col_step == 0):
                shift_by = -(row_step * GW + col_step)
                block_k, block_v = blocks_for(own_place + shift_by, slot_of(row_step, col_step))
                arrived[row_step, col_step] = shifted(
                    (
                        edge_part(key_grid, row_step, col_step),
                        edge_part(value_grid, row_step, col_step),
                        block_k,
                        block_v,
                    ),
                    "sp",
                    shift_by,
                )
    arrived[0, 0] = (key_grid, value_grid, center_k, center_v)
    bands_k = []
    bands_v = []
    for row_step in (-1, 0, 1):
        bands_k.append(
            jnp.concatenate([arrived[row_step, col_step][0] for col_step in (-1, 0, 1)], axis=2)
        )
        bands_v.append(
            jnp.concatenate([arrived[row_step, col_step][1] for col_step in (-1, 0, 1)], axis=2)
        )
    window_k = jnp.concatenate(bands_k, axis=1)
    window_v = jnp.concatenate(bands_v, axis=1)
    cache_list_k = []
    cache_list_v = []
    for row_step in (-1, 0, 1):
        for col_step in (-1, 0, 1):
            cache_list_k.append(arrived[row_step, col_step][2])
            cache_list_v.append(arrived[row_step, col_step][3])
    flat_wk = window_k.reshape(-1, channels)
    flat_wv = window_v.reshape(-1, channels)
    flat_ck = jnp.stack(cache_list_k).reshape(-1, channels)
    flat_cv = jnp.stack(cache_list_v).reshape(-1, channels)
    flat_q = query_normed.reshape(-1, channels)
    margins = window_margins[0]
    tile_row = own_place // GW
    tile_col = own_place % GW
    row_pos = jnp.arange(TH + 2 * HALO, dtype=jnp.int32)
    row_global = tile_row * TH - HALO + row_pos
    row_valid = (
        (row_global >= 0)
        & (row_global < grid_rows * TH)
        & (row_pos >= HALO - margins[0])
        & (row_pos < HALO + TH + margins[1])
    )
    col_pos = jnp.arange(TW + 2 * HALO, dtype=jnp.int32)
    col_global = tile_col * TW - HALO + col_pos
    col_valid = (
        (col_global >= 0)
        & (col_global < GW * TW)
        & (col_pos >= HALO - margins[2])
        & (col_pos < HALO + TW + margins[3])
    )
    window_valid = jnp.broadcast_to(
        (row_valid[:, None] & col_valid[None, :])[None], (frames_now, TH + 2 * HALO, TW + 2 * HALO)
    ).reshape(-1)
    own_listed = lax.dynamic_index_in_dim(cache_frames, own_place, 0, keepdims=False)
    cache_valid = jnp.broadcast_to(
        (own_listed >= 0)[:, :, None], (9, own_listed.shape[1], tile_len)
    ).reshape(-1)
    score_scale = HS ** (-0.5)

    head_count = channels // HS
    query_rows = flat_q.shape[0]
    window_len = flat_wk.shape[0]
    cache_len = flat_ck.shape[0]
    heads_out = pl.pallas_call(
        attend_kernel,
        grid=(head_count,),
        in_specs=[
            pl.BlockSpec((1, window_len), lambda h: (0, 0)),
            pl.BlockSpec((1, cache_len), lambda h: (0, 0)),
            pl.BlockSpec((query_rows, HS), lambda h: (0, h)),
            pl.BlockSpec((window_len, HS), lambda h: (0, h)),
            pl.BlockSpec((cache_len, HS), lambda h: (0, h)),
            pl.BlockSpec((window_len, HS), lambda h: (0, h)),
            pl.BlockSpec((cache_len, HS), lambda h: (0, h)),
        ],
        out_specs=pl.BlockSpec((query_rows, HS), lambda h: (0, h)),
        out_shape=jax.ShapeDtypeStruct((query_rows, channels), jnp.bfloat16),
        compiler_params=pltpu.CompilerParams(vmem_limit_bytes=60 * 1024 * 1024),
    )(
        window_valid.astype(jnp.int32)[None, :],
        cache_valid.astype(jnp.int32)[None, :],
        flat_q,
        flat_wk,
        flat_ck,
        flat_wv,
        flat_cv,
    )
    result = heads_out.reshape(1, frames_now, tile_len, channels)
    return result


def solution(mesh):
    return jax.shard_map(
        body,
        mesh=mesh,
        in_specs=(
            P("sp", None, None, "hd"),
            P("sp", None, None, "hd"),
            P("sp", None, None, "hd"),
            P("sp", None, None, "hd"),
            P("sp", None, None, "hd"),
            P("hd"),
            P("hd"),
            P("sp", None),
            P(),
        ),
        out_specs=P("sp", None, None, "hd"),
        check_vma=False,
    )
```

```python
import jax
import jax.numpy as jnp
from jax import lax
from jax.sharding import PartitionSpec as P
from jax.experimental import pallas as pl
from jax.experimental.pallas import tpu as pltpu

HS = 128
TH = 8
TW = 16
GW = 8
HALO = 4


EPSILON = 1e-06
MASKED = -1e30


def shifted(x, axis, by):
    size = lax.axis_size(axis)
    pairs = [(i, i + by) for i in range(size) if 0 <= i + by < size]
    return lax.ppermute(x, axis, pairs)


def edge_part(grid, row_step, col_step):
    if row_step == -1:
        grid = grid[:, TH - HALO :]
    elif row_step == 1:
        grid = grid[:, :HALO]
    if col_step == -1:
        grid = grid[:, :, TW - HALO :]
    elif col_step == 1:
        grid = grid[:, :, :HALO]
    return grid


def slot_of(row_step, col_step):
    return 3 * (row_step + 1) + (col_step + 1)


def normalize(tensor, gain, row_total, width_all):
    wide = tensor.astype(jnp.float32)
    factor = lax.rsqrt(row_total / width_all + EPSILON)
    return (wide * factor[..., None] * gain).astype(jnp.bfloat16)


def attend_kernel(wvalid_ref, cvalid_ref, q_ref, wk_ref, ck_ref, wv_ref, cv_ref, o_ref):
    score_scale = HS ** (-0.5)
    dims = (((1,), (1,)), ((), ()))
    head_q = q_ref[...]
    window_scores = (
        lax.dot_general(head_q, wk_ref[...], dims, preferred_element_type=jnp.float32)
        * score_scale
    )
    window_scores = jnp.where(wvalid_ref[...] > 0, window_scores, MASKED)
    cache_scores = (
        lax.dot_general(head_q, ck_ref[...], dims, preferred_element_type=jnp.float32)
        * score_scale
    )
    cache_scores = jnp.where(cvalid_ref[...] > 0, cache_scores, MASKED)
    row_top = jnp.maximum(
        jnp.max(window_scores, axis=1, keepdims=True), jnp.max(cache_scores, axis=1, keepdims=True)
    )
    window_exp = jnp.exp(window_scores - row_top)
    cache_exp = jnp.exp(cache_scores - row_top)
    row_total = jnp.sum(window_exp, axis=1, keepdims=True) + jnp.sum(
        cache_exp, axis=1, keepdims=True
    )
    window_probs = (window_exp / row_total).astype(jnp.bfloat16)
    cache_probs = (cache_exp / row_total).astype(jnp.bfloat16)
    mixed_out = jnp.dot(window_probs, wv_ref[...], preferred_element_type=jnp.float32) + jnp.dot(
        cache_probs, cv_ref[...], preferred_element_type=jnp.float32
    )
    o_ref[...] = mixed_out.astype(jnp.bfloat16)


def body(
    query, keys, values, cache_keys, cache_values, q_gain, k_gain, window_margins, cache_frames
):
    frames_now = query.shape[1]
    tile_len = query.shape[2]
    channels = query.shape[3]
    width_all = channels * lax.axis_size("hd")
    query_wide = query[0].astype(jnp.float32)
    keys_wide = keys[0].astype(jnp.float32)
    query_total, keys_total = lax.psum(
        (jnp.sum(query_wide * query_wide, axis=-1), jnp.sum(keys_wide * keys_wide, axis=-1)), "hd"
    )
    query_normed = normalize(query[0], q_gain, query_total, width_all)
    keys_normed = normalize(keys[0], k_gain, keys_total, width_all)
    key_grid = keys_normed.reshape(frames_now, TH, TW, channels)
    value_grid = values[0].reshape(frames_now, TH, TW, channels)
    own_place = lax.axis_index("sp")
    tile_count = lax.axis_size("sp")
    grid_rows = tile_count // GW
    own_cache_k = cache_keys[0]
    own_cache_v = cache_values[0]

    cap = cache_frames.shape[2]

    def blocks_for(target, slot_index):
        safe_target = jnp.clip(target, 0, tile_count - 1)
        listed = lax.dynamic_index_in_dim(cache_frames, safe_target, 0, keepdims=False)[slot_index]
        wanted = jnp.maximum(listed, 0)
        picked_k = [
            lax.dynamic_index_in_dim(own_cache_k, wanted[c], 0, keepdims=False) for c in range(cap)
        ]
        picked_v = [
            lax.dynamic_index_in_dim(own_cache_v, wanted[c], 0, keepdims=False) for c in range(cap)
        ]
        return picked_k, picked_v

    center_k, center_v = blocks_for(own_place, 4)
    center_k = jnp.stack(center_k)
    center_v = jnp.stack(center_v)
    arrived = {}
    for row_step in (-1, 0, 1):
        for col_step in (-1, 0, 1):
            if not (row_step == 0 and col_step == 0):
                shift_by = -(row_step * GW + col_step)
                block_k, block_v = blocks_for(own_place + shift_by, slot_of(row_step, col_step))
                edge_k = edge_part(key_grid, row_step, col_step)
                edge_v = edge_part(value_grid, row_step, col_step)
                edge_shape = edge_k.shape
                edge_rows = edge_k.size // channels
                packed = jnp.concatenate(
                    [edge_k.reshape(edge_rows, channels), edge_v.reshape(edge_rows, channels)]
                    + block_k
                    + block_v,
                    axis=0,
                )
                got = shifted(packed, "sp", shift_by)
                cache_rows = cap * tile_len
                arrived[row_step, col_step] = (
                    got[:edge_rows].reshape(edge_shape),
                    got[edge_rows : 2 * edge_rows].reshape(edge_shape),
                    got[2 * edge_rows : 2 * edge_rows + cache_rows].reshape(cap, tile_len, channels),
                    got[2 * edge_rows + cache_rows :].reshape(cap, tile_len, channels),
                )
    arrived[0, 0] = (key_grid, value_grid, center_k, center_v)
    bands_k = []
    bands_v = []
    for row_step in (-1, 0, 1):
        bands_k.append(
            jnp.concatenate([arrived[row_step, col_step][0] for col_step in (-1, 0, 1)], axis=2)
        )
        bands_v.append(
            jnp.concatenate([arrived[row_step, col_step][1] for col_step in (-1, 0, 1)], axis=2)
        )
    window_k = jnp.concatenate(bands_k, axis=1)
    window_v = jnp.concatenate(bands_v, axis=1)
    cache_list_k = []
    cache_list_v = []
    for row_step in (-1, 0, 1):
        for col_step in (-1, 0, 1):
            cache_list_k.append(arrived[row_step, col_step][2])
            cache_list_v.append(arrived[row_step, col_step][3])
    flat_wk = window_k.reshape(-1, channels)
    flat_wv = window_v.reshape(-1, channels)
    flat_ck = jnp.stack(cache_list_k).reshape(-1, channels)
    flat_cv = jnp.stack(cache_list_v).reshape(-1, channels)
    flat_q = query_normed.reshape(-1, channels)
    margins = window_margins[0]
    tile_row = own_place // GW
    tile_col = own_place % GW
    row_pos = jnp.arange(TH + 2 * HALO, dtype=jnp.int32)
    row_global = tile_row * TH - HALO + row_pos
    row_valid = (
        (row_global >= 0)
        & (row_global < grid_rows * TH)
        & (row_pos >= HALO - margins[0])
        & (row_pos < HALO + TH + margins[1])
    )
    col_pos = jnp.arange(TW + 2 * HALO, dtype=jnp.int32)
    col_global = tile_col * TW - HALO + col_pos
    col_valid = (
        (col_global >= 0)
        & (col_global < GW * TW)
        & (col_pos >= HALO - margins[2])
        & (col_pos < HALO + TW + margins[3])
    )
    window_valid = jnp.broadcast_to(
        (row_valid[:, None] & col_valid[None, :])[None], (frames_now, TH + 2 * HALO, TW + 2 * HALO)
    ).reshape(-1)
    own_listed = lax.dynamic_index_in_dim(cache_frames, own_place, 0, keepdims=False)
    cache_valid = jnp.broadcast_to(
        (own_listed >= 0)[:, :, None], (9, own_listed.shape[1], tile_len)
    ).reshape(-1)
    score_scale = HS ** (-0.5)

    head_count = channels // HS
    query_rows = flat_q.shape[0]
    window_len = flat_wk.shape[0]
    cache_len = flat_ck.shape[0]
    heads_out = pl.pallas_call(
        attend_kernel,
        grid=(head_count,),
        in_specs=[
            pl.BlockSpec((1, window_len), lambda h: (0, 0)),
            pl.BlockSpec((1, cache_len), lambda h: (0, 0)),
            pl.BlockSpec((query_rows, HS), lambda h: (0, h)),
            pl.BlockSpec((window_len, HS), lambda h: (0, h)),
            pl.BlockSpec((cache_len, HS), lambda h: (0, h)),
            pl.BlockSpec((window_len, HS), lambda h: (0, h)),
            pl.BlockSpec((cache_len, HS), lambda h: (0, h)),
        ],
        out_specs=pl.BlockSpec((query_rows, HS), lambda h: (0, h)),
        out_shape=jax.ShapeDtypeStruct((query_rows, channels), jnp.bfloat16),
        compiler_params=pltpu.CompilerParams(vmem_limit_bytes=60 * 1024 * 1024),
    )(
        window_valid.astype(jnp.int32)[None, :],
        cache_valid.astype(jnp.int32)[None, :],
        flat_q,
        flat_wk,
        flat_ck,
        flat_wv,
        flat_cv,
    )
    result = heads_out.reshape(1, frames_now, tile_len, channels)
    return result


def solution(mesh):
    return jax.shard_map(
        body,
        mesh=mesh,
        in_specs=(
            P("sp", None, None, "hd"),
            P("sp", None, None, "hd"),
            P("sp", None, None, "hd"),
            P("sp", None, None, "hd"),
            P("sp", None, None, "hd"),
            P("hd"),
            P("hd"),
            P("sp", None),
            P(),
        ),
        out_specs=P("sp", None, None, "hd"),
        check_vma=False,
    )
```

```python
import jax
import jax.numpy as jnp
from jax import lax
from jax.sharding import PartitionSpec as P
from jax.experimental import pallas as pl
from jax.experimental.pallas import tpu as pltpu

HS = 128
TH = 8
TW = 16
GW = 8
HALO = 4


EPSILON = 1e-06
MASKED = -1e30
STEPS = [(r, c) for r in (-1, 0, 1) for c in (-1, 0, 1)]


def shifted(x, axis, by):
    size = lax.axis_size(axis)
    pairs = [(i, i + by) for i in range(size) if 0 <= i + by < size]
    return lax.ppermute(x, axis, pairs)


def edge_part(grid, row_step, col_step):
    if row_step == -1:
        grid = grid[:, :, TH - HALO :]
    elif row_step == 1:
        grid = grid[:, :, :HALO]
    if col_step == -1:
        grid = grid[:, :, :, TW - HALO :]
    elif col_step == 1:
        grid = grid[:, :, :, :HALO]
    return grid


def slot_of(row_step, col_step):
    return 3 * (row_step + 1) + (col_step + 1)


def normalize(tensor, gain, row_total, width_all):
    wide = tensor.astype(jnp.float32)
    factor = lax.rsqrt(row_total / width_all + EPSILON)
    return (wide * factor[..., None] * gain).astype(jnp.bfloat16)


def attend_kernel(wvalid_ref, cvalid_ref, q_ref, wk_ref, wv_ref, *rest):
    cache_refs = rest[:-1]
    o_ref = rest[-1]
    cap_rows = cache_refs[0].shape[0] // 2
    tile_len = cache_refs[0].shape[1]
    score_scale = HS ** (-0.5)
    dims = (((1,), (1,)), ((), ()))
    head_q = q_ref[...]
    cache_k = jnp.concatenate(
        [ref[:cap_rows].reshape(cap_rows * tile_len, HS) for ref in cache_refs], axis=0
    )
    cache_v = jnp.concatenate(
        [ref[cap_rows:].reshape(cap_rows * tile_len, HS) for ref in cache_refs], axis=0
    )
    window_scores = (
        lax.dot_general(head_q, wk_ref[...], dims, preferred_element_type=jnp.float32)
        * score_scale
    )
    window_scores = jnp.where(wvalid_ref[...] > 0, window_scores, MASKED)
    cache_scores = (
        lax.dot_general(head_q, cache_k, dims, preferred_element_type=jnp.float32) * score_scale
    )
    cache_scores = jnp.where(cvalid_ref[...] > 0, cache_scores, MASKED)
    row_top = jnp.maximum(
        jnp.max(window_scores, axis=1, keepdims=True), jnp.max(cache_scores, axis=1, keepdims=True)
    )
    window_exp = jnp.exp(window_scores - row_top)
    cache_exp = jnp.exp(cache_scores - row_top)
    row_total = jnp.sum(window_exp, axis=1, keepdims=True) + jnp.sum(
        cache_exp, axis=1, keepdims=True
    )
    window_probs = (window_exp / row_total).astype(jnp.bfloat16)
    cache_probs = (cache_exp / row_total).astype(jnp.bfloat16)
    mixed_out = jnp.dot(window_probs, wv_ref[...], preferred_element_type=jnp.float32) + jnp.dot(
        cache_probs, cache_v, preferred_element_type=jnp.float32
    )
    o_ref[...] = mixed_out.astype(jnp.bfloat16)


def body(
    query, keys, values, cache_keys, cache_values, q_gain, k_gain, window_margins, cache_frames
):
    frames_now = query.shape[1]
    tile_len = query.shape[2]
    channels = query.shape[3]
    width_all = channels * lax.axis_size("hd")
    own_place = lax.axis_index("sp")
    tile_count = lax.axis_size("sp")
    grid_rows = tile_count // GW
    own_cache_k = cache_keys[0]
    own_cache_v = cache_values[0]
    cap = cache_frames.shape[2]

    def blocks_for(target, slot_index):
        safe_target = jnp.clip(target, 0, tile_count - 1)
        listed = lax.dynamic_index_in_dim(cache_frames, safe_target, 0, keepdims=False)[slot_index]
        wanted = jnp.maximum(listed, 0)
        picked = [
            lax.dynamic_index_in_dim(own_cache_k, wanted[c], 0, keepdims=False) for c in range(cap)
        ] + [
            lax.dynamic_index_in_dim(own_cache_v, wanted[c], 0, keepdims=False) for c in range(cap)
        ]
        return jnp.stack(picked)

    cache_in = {}
    for row_step, col_step in STEPS:
        if (row_step, col_step) != (0, 0):
            shift_by = -(row_step * GW + col_step)
            packed = blocks_for(own_place + shift_by, slot_of(row_step, col_step))
            cache_in[row_step, col_step] = shifted(packed, "sp", shift_by)
    cache_in[0, 0] = blocks_for(own_place, 4)

    query_wide = query[0].astype(jnp.float32)
    keys_wide = keys[0].astype(jnp.float32)
    query_total, keys_total = lax.psum(
        (jnp.sum(query_wide * query_wide, axis=-1), jnp.sum(keys_wide * keys_wide, axis=-1)),
        "hd",
    )
    query_normed = normalize(query[0], q_gain, query_total, width_all)
    keys_normed = normalize(keys[0], k_gain, keys_total, width_all)
    key_grid = keys_normed.reshape(frames_now, TH, TW, channels)
    value_grid = values[0].reshape(frames_now, TH, TW, channels)
    both_grid = jnp.stack([key_grid, value_grid])

    edge_in = {}
    for row_step, col_step in STEPS:
        if (row_step, col_step) != (0, 0):
            shift_by = -(row_step * GW + col_step)
            edge_in[row_step, col_step] = shifted(
                edge_part(both_grid, row_step, col_step), "sp", shift_by
            )
    edge_in[0, 0] = both_grid
    bands = []
    for row_step in (-1, 0, 1):
        bands.append(
            jnp.concatenate([edge_in[row_step, col_step] for col_step in (-1, 0, 1)], axis=3)
        )
    window = jnp.concatenate(bands, axis=2)
    flat_wk = window[0].reshape(-1, channels)
    flat_wv = window[1].reshape(-1, channels)
    flat_q = query_normed.reshape(-1, channels)
    margins = window_margins[0]
    tile_row = own_place // GW
    tile_col = own_place % GW
    row_pos = jnp.arange(TH + 2 * HALO, dtype=jnp.int32)
    row_global = tile_row * TH - HALO + row_pos
    row_valid = (
        (row_global >= 0)
        & (row_global < grid_rows * TH)
        & (row_pos >= HALO - margins[0])
        & (row_pos < HALO + TH + margins[1])
    )
    col_pos = jnp.arange(TW + 2 * HALO, dtype=jnp.int32)
    col_global = tile_col * TW - HALO + col_pos
    col_valid = (
        (col_global >= 0)
        & (col_global < GW * TW)
        & (col_pos >= HALO - margins[2])
        & (col_pos < HALO + TW + margins[3])
    )
    window_valid = jnp.broadcast_to(
        (row_valid[:, None] & col_valid[None, :])[None], (frames_now, TH + 2 * HALO, TW + 2 * HALO)
    ).reshape(-1)
    own_listed = lax.dynamic_index_in_dim(cache_frames, own_place, 0, keepdims=False)
    cache_valid = jnp.broadcast_to(
        (own_listed >= 0)[:, :, None], (9, own_listed.shape[1], tile_len)
    ).reshape(-1)

    head_count = channels // HS
    query_rows = flat_q.shape[0]
    window_len = flat_wk.shape[0]
    cache_len = cache_valid.shape[0]
    cache_list = [cache_in[step] for step in STEPS]
    heads_out = pl.pallas_call(
        attend_kernel,
        grid=(head_count,),
        in_specs=[
            pl.BlockSpec((1, window_len), lambda h: (0, 0)),
            pl.BlockSpec((1, cache_len), lambda h: (0, 0)),
            pl.BlockSpec((query_rows, HS), lambda h: (0, h)),
            pl.BlockSpec((window_len, HS), lambda h: (0, h)),
            pl.BlockSpec((window_len, HS), lambda h: (0, h)),
        ]
        + [pl.BlockSpec((2 * cap, tile_len, HS), lambda h: (0, 0, h)) for _ in cache_list],
        out_specs=pl.BlockSpec((query_rows, HS), lambda h: (0, h)),
        out_shape=jax.ShapeDtypeStruct((query_rows, channels), jnp.bfloat16),
        compiler_params=pltpu.CompilerParams(vmem_limit_bytes=60 * 1024 * 1024),
    )(
        window_valid.astype(jnp.int32)[None, :],
        cache_valid.astype(jnp.int32)[None, :],
        flat_q,
        flat_wk,
        flat_wv,
        *cache_list,
    )
    result = heads_out.reshape(1, frames_now, tile_len, channels)
    return result


def solution(mesh):
    return jax.shard_map(
        body,
        mesh=mesh,
        in_specs=(
            P("sp", None, None, "hd"),
            P("sp", None, None, "hd"),
            P("sp", None, None, "hd"),
            P("sp", None, None, "hd"),
            P("sp", None, None, "hd"),
            P("hd"),
            P("hd"),
            P("sp", None),
            P(),
        ),
        out_specs=P("sp", None, None, "hd"),
        check_vma=False,
    )
```

```python
import jax
import jax.numpy as jnp
from jax import lax
from jax.sharding import PartitionSpec as P
from jax.experimental import pallas as pl
from jax.experimental.pallas import tpu as pltpu

HS = 128
TH = 8
TW = 16
GW = 8
HALO = 4


EPSILON = 1e-06
MASKED = -1e30
STEPS = [(r, c) for r in (-1, 0, 1) for c in (-1, 0, 1)]


def shifted(x, axis, by):
    size = lax.axis_size(axis)
    pairs = [(i, i + by) for i in range(size) if 0 <= i + by < size]
    return lax.ppermute(x, axis, pairs)


def edge_part(grid, row_step, col_step):
    if row_step == -1:
        grid = grid[:, :, TH - HALO :]
    elif row_step == 1:
        grid = grid[:, :, :HALO]
    if col_step == -1:
        grid = grid[:, :, :, TW - HALO :]
    elif col_step == 1:
        grid = grid[:, :, :, :HALO]
    return grid


def slot_of(row_step, col_step):
    return 3 * (row_step + 1) + (col_step + 1)


def normalize(tensor, gain, row_total, width_all):
    wide = tensor.astype(jnp.float32)
    factor = lax.rsqrt(row_total / width_all + EPSILON)
    return (wide * factor[..., None] * gain).astype(jnp.bfloat16)


def attend_kernel(wvalid_ref, cvalid_ref, q_ref, wk_ref, wv_ref, *rest):
    cache_refs = rest[:-1]
    o_ref = rest[-1]
    cap_rows = cache_refs[0].shape[0] // 2
    tile_len = cache_refs[0].shape[1]
    score_scale = HS ** (-0.5)
    dims = (((1,), (1,)), ((), ()))
    head_q = q_ref[...]
    cache_k = jnp.concatenate(
        [ref[:cap_rows].reshape(cap_rows * tile_len, HS) for ref in cache_refs], axis=0
    )
    cache_v = jnp.concatenate(
        [ref[cap_rows:].reshape(cap_rows * tile_len, HS) for ref in cache_refs], axis=0
    )
    window_scores = (
        lax.dot_general(head_q, wk_ref[...], dims, preferred_element_type=jnp.float32)
        * score_scale
    )
    window_scores = jnp.where(wvalid_ref[...] > 0, window_scores, MASKED)
    cache_scores = (
        lax.dot_general(head_q, cache_k, dims, preferred_element_type=jnp.float32) * score_scale
    )
    cache_scores = jnp.where(cvalid_ref[...] > 0, cache_scores, MASKED)
    row_top = jnp.maximum(
        jnp.max(window_scores, axis=1, keepdims=True), jnp.max(cache_scores, axis=1, keepdims=True)
    )
    window_exp = jnp.exp(window_scores - row_top)
    cache_exp = jnp.exp(cache_scores - row_top)
    row_total = jnp.sum(window_exp, axis=1, keepdims=True) + jnp.sum(
        cache_exp, axis=1, keepdims=True
    )
    window_probs = (window_exp / row_total).astype(jnp.bfloat16)
    cache_probs = (cache_exp / row_total).astype(jnp.bfloat16)
    mixed_out = jnp.dot(window_probs, wv_ref[...], preferred_element_type=jnp.float32) + jnp.dot(
        cache_probs, cache_v, preferred_element_type=jnp.float32
    )
    o_ref[...] = mixed_out.astype(jnp.bfloat16)


def pick_kernel(idx_ref, k0_ref, k1_ref, v0_ref, v1_ref, o_ref):
    o_ref[0, 0] = k0_ref[0]
    o_ref[0, 1] = k1_ref[0]
    o_ref[0, 2] = v0_ref[0]
    o_ref[0, 3] = v1_ref[0]


def body(
    query, keys, values, cache_keys, cache_values, q_gain, k_gain, window_margins, cache_frames
):
    frames_now = query.shape[1]
    tile_len = query.shape[2]
    channels = query.shape[3]
    width_all = channels * lax.axis_size("hd")
    own_place = lax.axis_index("sp")
    tile_count = lax.axis_size("sp")
    grid_rows = tile_count // GW
    own_cache_k = cache_keys[0]
    own_cache_v = cache_values[0]
    cap = cache_frames.shape[2]

    slot_ids = jnp.arange(9, dtype=jnp.int32)
    targets = jnp.clip(
        own_place - ((slot_ids // 3 - 1) * GW + (slot_ids % 3 - 1)), 0, tile_count - 1
    )
    listed = cache_frames[targets, slot_ids]
    wanted = jnp.clip(listed, 0, own_cache_k.shape[0] - 1).reshape(-1).astype(jnp.int32)
    block_shape = (1,) + own_cache_k.shape[1:]
    picked = pl.pallas_call(
        pick_kernel,
        grid_spec=pltpu.PrefetchScalarGridSpec(
            num_scalar_prefetch=1,
            grid=(9,),
            in_specs=[
                pl.BlockSpec(block_shape, lambda d, idx: (idx[2 * d], 0, 0)),
                pl.BlockSpec(block_shape, lambda d, idx: (idx[2 * d + 1], 0, 0)),
                pl.BlockSpec(block_shape, lambda d, idx: (idx[2 * d], 0, 0)),
                pl.BlockSpec(block_shape, lambda d, idx: (idx[2 * d + 1], 0, 0)),
            ],
            out_specs=pl.BlockSpec((1, 2 * cap) + own_cache_k.shape[1:], lambda d, idx: (d, 0, 0, 0)),
        ),
        out_shape=jax.ShapeDtypeStruct((9, 2 * cap) + own_cache_k.shape[1:], own_cache_k.dtype),
    )(wanted, own_cache_k, own_cache_k, own_cache_v, own_cache_v)

    cache_in = {}
    for row_step, col_step in STEPS:
        slot = slot_of(row_step, col_step)
        if (row_step, col_step) != (0, 0):
            shift_by = -(row_step * GW + col_step)
            cache_in[row_step, col_step] = shifted(picked[slot], "sp", shift_by)
        else:
            cache_in[row_step, col_step] = picked[slot]

    query_wide = query[0].astype(jnp.float32)
    keys_wide = keys[0].astype(jnp.float32)
    query_total, keys_total = lax.psum(
        (jnp.sum(query_wide * query_wide, axis=-1), jnp.sum(keys_wide * keys_wide, axis=-1)),
        "hd",
    )
    query_normed = normalize(query[0], q_gain, query_total, width_all)
    keys_normed = normalize(keys[0], k_gain, keys_total, width_all)
    key_grid = keys_normed.reshape(frames_now, TH, TW, channels)
    value_grid = values[0].reshape(frames_now, TH, TW, channels)
    both_grid = jnp.stack([key_grid, value_grid])

    edge_in = {}
    for row_step, col_step in STEPS:
        if (row_step, col_step) != (0, 0):
            shift_by = -(row_step * GW + col_step)
            edge_in[row_step, col_step] = shifted(
                edge_part(both_grid, row_step, col_step), "sp", shift_by
            )
    edge_in[0, 0] = both_grid
    bands = []
    for row_step in (-1, 0, 1):
        bands.append(
            jnp.concatenate([edge_in[row_step, col_step] for col_step in (-1, 0, 1)], axis=3)
        )
    window = jnp.concatenate(bands, axis=2)
    flat_wk = window[0].reshape(-1, channels)
    flat_wv = window[1].reshape(-1, channels)
    flat_q = query_normed.reshape(-1, channels)
    margins = window_margins[0]
    tile_row = own_place // GW
    tile_col = own_place % GW
    row_pos = jnp.arange(TH + 2 * HALO, dtype=jnp.int32)
    row_global = tile_row * TH - HALO + row_pos
    row_valid = (
        (row_global >= 0)
        & (row_global < grid_rows * TH)
        & (row_pos >= HALO - margins[0])
        & (row_pos < HALO + TH + margins[1])
    )
    col_pos = jnp.arange(TW + 2 * HALO, dtype=jnp.int32)
    col_global = tile_col * TW - HALO + col_pos
    col_valid = (
        (col_global >= 0)
        & (col_global < GW * TW)
        & (col_pos >= HALO - margins[2])
        & (col_pos < HALO + TW + margins[3])
    )
    window_valid = jnp.broadcast_to(
        (row_valid[:, None] & col_valid[None, :])[None], (frames_now, TH + 2 * HALO, TW + 2 * HALO)
    ).reshape(-1)
    own_listed = lax.dynamic_index_in_dim(cache_frames, own_place, 0, keepdims=False)
    cache_valid = jnp.broadcast_to(
        (own_listed >= 0)[:, :, None], (9, own_listed.shape[1], tile_len)
    ).reshape(-1)

    head_count = channels // HS
    query_rows = flat_q.shape[0]
    window_len = flat_wk.shape[0]
    cache_len = cache_valid.shape[0]
    cache_list = [cache_in[step] for step in STEPS]
    heads_out = pl.pallas_call(
        attend_kernel,
        grid=(head_count,),
        in_specs=[
            pl.BlockSpec((1, window_len), lambda h: (0, 0)),
            pl.BlockSpec((1, cache_len), lambda h: (0, 0)),
            pl.BlockSpec((query_rows, HS), lambda h: (0, h)),
            pl.BlockSpec((window_len, HS), lambda h: (0, h)),
            pl.BlockSpec((window_len, HS), lambda h: (0, h)),
        ]
        + [pl.BlockSpec((2 * cap, tile_len, HS), lambda h: (0, 0, h)) for _ in cache_list],
        out_specs=pl.BlockSpec((query_rows, HS), lambda h: (0, h)),
        out_shape=jax.ShapeDtypeStruct((query_rows, channels), jnp.bfloat16),
        compiler_params=pltpu.CompilerParams(vmem_limit_bytes=60 * 1024 * 1024),
    )(
        window_valid.astype(jnp.int32)[None, :],
        cache_valid.astype(jnp.int32)[None, :],
        flat_q,
        flat_wk,
        flat_wv,
        *cache_list,
    )
    result = heads_out.reshape(1, frames_now, tile_len, channels)
    return result


def solution(mesh):
    return jax.shard_map(
        body,
        mesh=mesh,
        in_specs=(
            P("sp", None, None, "hd"),
            P("sp", None, None, "hd"),
            P("sp", None, None, "hd"),
            P("sp", None, None, "hd"),
            P("sp", None, None, "hd"),
            P("hd"),
            P("hd"),
            P("sp", None),
            P(),
        ),
        out_specs=P("sp", None, None, "hd"),
        check_vma=False,
    )
```

```python
import jax
import jax.numpy as jnp
from jax import lax
from jax.sharding import PartitionSpec as P
from jax.experimental import pallas as pl
from jax.experimental.pallas import tpu as pltpu

HS = 128
TH = 8
TW = 16
GW = 8
HALO = 4


EPSILON = 1e-06
MASKED = -1e30
STEPS = [(r, c) for r in (-1, 0, 1) for c in (-1, 0, 1)]


def shifted(x, axis, by):
    size = lax.axis_size(axis)
    pairs = [(i, i + by) for i in range(size) if 0 <= i + by < size]
    return lax.ppermute(x, axis, pairs)


def edge_part(grid, row_step, col_step):
    if row_step == -1:
        grid = grid[:, :, TH - HALO :]
    elif row_step == 1:
        grid = grid[:, :, :HALO]
    if col_step == -1:
        grid = grid[:, :, :, TW - HALO :]
    elif col_step == 1:
        grid = grid[:, :, :, :HALO]
    return grid


def hd_sum(x):
    size = lax.axis_size("hd")
    step = 1
    while step < size:
        pairs = [(i, i ^ step) for i in range(size)]
        x = x + lax.ppermute(x, "hd", pairs)
        step *= 2
    return x


def slot_of(row_step, col_step):
    return 3 * (row_step + 1) + (col_step + 1)


def normalize(tensor, gain, row_total, width_all):
    wide = tensor.astype(jnp.float32)
    factor = lax.rsqrt(row_total / width_all + EPSILON)
    return (wide * factor[..., None] * gain).astype(jnp.bfloat16)


def attend_kernel(wvalid_ref, cvalid_ref, q_ref, wk_ref, wv_ref, *rest):
    cache_refs = rest[:-1]
    o_ref = rest[-1]
    cap_rows = cache_refs[0].shape[0] // 2
    tile_len = cache_refs[0].shape[1]
    score_scale = HS ** (-0.5)
    dims = (((1,), (1,)), ((), ()))
    head_q = q_ref[...]
    cache_k = jnp.concatenate(
        [ref[:cap_rows].reshape(cap_rows * tile_len, HS) for ref in cache_refs], axis=0
    )
    cache_v = jnp.concatenate(
        [ref[cap_rows:].reshape(cap_rows * tile_len, HS) for ref in cache_refs], axis=0
    )
    window_scores = (
        lax.dot_general(head_q, wk_ref[...], dims, preferred_element_type=jnp.float32)
        * score_scale
    )
    window_scores = jnp.where(wvalid_ref[...] > 0, window_scores, MASKED)
    cache_scores = (
        lax.dot_general(head_q, cache_k, dims, preferred_element_type=jnp.float32) * score_scale
    )
    cache_scores = jnp.where(cvalid_ref[...] > 0, cache_scores, MASKED)
    row_top = jnp.maximum(
        jnp.max(window_scores, axis=1, keepdims=True), jnp.max(cache_scores, axis=1, keepdims=True)
    )
    window_exp = jnp.exp(window_scores - row_top)
    cache_exp = jnp.exp(cache_scores - row_top)
    row_total = jnp.sum(window_exp, axis=1, keepdims=True) + jnp.sum(
        cache_exp, axis=1, keepdims=True
    )
    row_scale = 1.0 / row_total
    window_probs = (window_exp * row_scale).astype(jnp.bfloat16)
    cache_probs = (cache_exp * row_scale).astype(jnp.bfloat16)
    mixed_out = jnp.dot(window_probs, wv_ref[...], preferred_element_type=jnp.float32) + jnp.dot(
        cache_probs, cache_v, preferred_element_type=jnp.float32
    )
    o_ref[...] = mixed_out.astype(jnp.bfloat16)


def pick_kernel(idx_ref, k_ref, v_ref, *o_refs):
    cap = o_refs[0].shape[0] // 2
    for d, o_ref in enumerate(o_refs):
        for c in range(cap):
            o_ref[c] = k_ref[idx_ref[cap * d + c]]
            o_ref[cap + c] = v_ref[idx_ref[cap * d + c]]


def body(
    query, keys, values, cache_keys, cache_values, q_gain, k_gain, window_margins, cache_frames
):
    frames_now = query.shape[1]
    tile_len = query.shape[2]
    channels = query.shape[3]
    width_all = channels * lax.axis_size("hd")
    own_place = lax.axis_index("sp")
    tile_count = lax.axis_size("sp")
    grid_rows = tile_count // GW
    own_cache_k = cache_keys[0]
    own_cache_v = cache_values[0]
    cap = cache_frames.shape[2]

    slot_ids = jnp.arange(9, dtype=jnp.int32)
    targets = jnp.clip(
        own_place - ((slot_ids // 3 - 1) * GW + (slot_ids % 3 - 1)), 0, tile_count - 1
    )
    listed = cache_frames[targets, slot_ids]
    wanted = jnp.clip(listed, 0, own_cache_k.shape[0] - 1).reshape(-1).astype(jnp.int32)
    full_spec = pl.BlockSpec(own_cache_k.shape, lambda i, idx: (0, 0, 0))
    out_block = (2 * cap,) + own_cache_k.shape[1:]
    picked = pl.pallas_call(
        pick_kernel,
        grid_spec=pltpu.PrefetchScalarGridSpec(
            num_scalar_prefetch=1,
            grid=(1,),
            in_specs=[full_spec, full_spec],
            out_specs=[pl.BlockSpec(out_block, lambda i, idx: (0, 0, 0)) for _ in range(9)],
        ),
        out_shape=[jax.ShapeDtypeStruct(out_block, own_cache_k.dtype) for _ in range(9)],
    )(wanted, own_cache_k, own_cache_v)

    cache_in = {}
    for row_step, col_step in STEPS:
        slot = slot_of(row_step, col_step)
        if (row_step, col_step) != (0, 0):
            shift_by = -(row_step * GW + col_step)
            cache_in[row_step, col_step] = shifted(picked[slot], "sp", shift_by)
        else:
            cache_in[row_step, col_step] = picked[slot]

    query_wide = query[0].astype(jnp.float32)
    keys_wide = keys[0].astype(jnp.float32)
    query_total, keys_total = hd_sum(
        jnp.stack(
            [jnp.sum(query_wide * query_wide, axis=-1), jnp.sum(keys_wide * keys_wide, axis=-1)]
        )
    )
    query_normed = normalize(query[0], q_gain, query_total, width_all)
    keys_normed = normalize(keys[0], k_gain, keys_total, width_all)
    key_grid = keys_normed.reshape(frames_now, TH, TW, channels)
    value_grid = values[0].reshape(frames_now, TH, TW, channels)
    both_grid = jnp.stack([key_grid, value_grid])

    edge_in = {}
    for row_step, col_step in STEPS:
        if (row_step, col_step) != (0, 0):
            shift_by = -(row_step * GW + col_step)
            edge_in[row_step, col_step] = shifted(
                edge_part(both_grid, row_step, col_step), "sp", shift_by
            )
    edge_in[0, 0] = both_grid
    bands = []
    for row_step in (-1, 0, 1):
        bands.append(
            jnp.concatenate([edge_in[row_step, col_step] for col_step in (-1, 0, 1)], axis=3)
        )
    window = jnp.concatenate(bands, axis=2)
    flat_wk = window[0].reshape(-1, channels)
    flat_wv = window[1].reshape(-1, channels)
    flat_q = query_normed.reshape(-1, channels)
    margins = window_margins[0]
    tile_row = own_place // GW
    tile_col = own_place % GW
    row_pos = jnp.arange(TH + 2 * HALO, dtype=jnp.int32)
    row_global = tile_row * TH - HALO + row_pos
    row_valid = (
        (row_global >= 0)
        & (row_global < grid_rows * TH)
        & (row_pos >= HALO - margins[0])
        & (row_pos < HALO + TH + margins[1])
    )
    col_pos = jnp.arange(TW + 2 * HALO, dtype=jnp.int32)
    col_global = tile_col * TW - HALO + col_pos
    col_valid = (
        (col_global >= 0)
        & (col_global < GW * TW)
        & (col_pos >= HALO - margins[2])
        & (col_pos < HALO + TW + margins[3])
    )
    window_valid = jnp.broadcast_to(
        (row_valid[:, None] & col_valid[None, :])[None], (frames_now, TH + 2 * HALO, TW + 2 * HALO)
    ).reshape(-1)
    own_listed = lax.dynamic_index_in_dim(cache_frames, own_place, 0, keepdims=False)
    cache_valid = jnp.broadcast_to(
        (own_listed >= 0)[:, :, None], (9, own_listed.shape[1], tile_len)
    ).reshape(-1)

    head_count = channels // HS
    query_rows = flat_q.shape[0]
    window_len = flat_wk.shape[0]
    cache_len = cache_valid.shape[0]
    cache_list = [cache_in[step] for step in STEPS]
    heads_out = pl.pallas_call(
        attend_kernel,
        grid=(head_count,),
        in_specs=[
            pl.BlockSpec((1, window_len), lambda h: (0, 0)),
            pl.BlockSpec((1, cache_len), lambda h: (0, 0)),
            pl.BlockSpec((query_rows, HS), lambda h: (0, h)),
            pl.BlockSpec((window_len, HS), lambda h: (0, h)),
            pl.BlockSpec((window_len, HS), lambda h: (0, h)),
        ]
        + [pl.BlockSpec((2 * cap, tile_len, HS), lambda h: (0, 0, h)) for _ in cache_list],
        out_specs=pl.BlockSpec((query_rows, HS), lambda h: (0, h)),
        out_shape=jax.ShapeDtypeStruct((query_rows, channels), jnp.bfloat16),
        compiler_params=pltpu.CompilerParams(vmem_limit_bytes=60 * 1024 * 1024),
    )(
        window_valid.astype(jnp.int32)[None, :],
        cache_valid.astype(jnp.int32)[None, :],
        flat_q,
        flat_wk,
        flat_wv,
        *cache_list,
    )
    result = heads_out.reshape(1, frames_now, tile_len, channels)
    return result


def solution(mesh):
    return jax.shard_map(
        body,
        mesh=mesh,
        in_specs=(
            P("sp", None, None, "hd"),
            P("sp", None, None, "hd"),
            P("sp", None, None, "hd"),
            P("sp", None, None, "hd"),
            P("sp", None, None, "hd"),
            P("hd"),
            P("hd"),
            P("sp", None),
            P(),
        ),
        out_specs=P("sp", None, None, "hd"),
        check_vma=False,
    )
```

```python
import jax
import jax.numpy as jnp
from jax import lax
from jax.sharding import PartitionSpec as P
from jax.experimental import pallas as pl
from jax.experimental.pallas import tpu as pltpu

HS = 128
TH = 8
TW = 16
GW = 8
HALO = 4


EPSILON = 1e-06
MASKED = -1e30
STEPS = [(r, c) for r in (-1, 0, 1) for c in (-1, 0, 1)]


def shifted(x, axis, by):
    size = lax.axis_size(axis)
    pairs = [(i, i + by) for i in range(size) if 0 <= i + by < size]
    return lax.ppermute(x, axis, pairs)


def edge_part(grid, row_step, col_step):
    if row_step == -1:
        grid = grid[:, :, TH - HALO :]
    elif row_step == 1:
        grid = grid[:, :, :HALO]
    if col_step == -1:
        grid = grid[:, :, :, TW - HALO :]
    elif col_step == 1:
        grid = grid[:, :, :, :HALO]
    return grid


def hd_sum(x):
    size = lax.axis_size("hd")
    step = 1
    while step < size:
        pairs = [(i, i ^ step) for i in range(size)]
        x = x + lax.ppermute(x, "hd", pairs)
        step *= 2
    return x


def slot_of(row_step, col_step):
    return 3 * (row_step + 1) + (col_step + 1)


def normalize(tensor, gain, row_total, width_all):
    wide = tensor.astype(jnp.float32)
    factor = lax.rsqrt(row_total / width_all + EPSILON)
    return (wide * factor[..., None] * gain).astype(jnp.bfloat16)


def window_kernel(wvalid_ref, cvalid_ref, q_ref, wk_ref, wv_ref, c_ref, acc_ref, m_ref, l_ref):
    cap_rows = c_ref.shape[0] // 2
    tile_len = c_ref.shape[1]
    score_scale = HS ** (-0.5)
    dims = (((1,), (1,)), ((), ()))
    head_q = q_ref[...]
    cache_k = c_ref[:cap_rows].reshape(cap_rows * tile_len, HS)
    cache_v = c_ref[cap_rows:].reshape(cap_rows * tile_len, HS)
    window_scores = (
        lax.dot_general(head_q, wk_ref[...], dims, preferred_element_type=jnp.float32)
        * score_scale
    )
    window_scores = jnp.where(wvalid_ref[...] > 0, window_scores, MASKED)
    cache_scores = (
        lax.dot_general(head_q, cache_k, dims, preferred_element_type=jnp.float32) * score_scale
    )
    cache_scores = jnp.where(cvalid_ref[...] > 0, cache_scores, MASKED)
    row_top = jnp.maximum(
        jnp.max(window_scores, axis=1, keepdims=True), jnp.max(cache_scores, axis=1, keepdims=True)
    )
    window_exp = jnp.exp(window_scores - row_top)
    cache_exp = jnp.exp(cache_scores - row_top)
    row_total = jnp.sum(window_exp, axis=1, keepdims=True) + jnp.sum(
        cache_exp, axis=1, keepdims=True
    )
    acc_ref[...] = jnp.dot(
        window_exp.astype(jnp.bfloat16), wv_ref[...], preferred_element_type=jnp.float32
    ) + jnp.dot(cache_exp.astype(jnp.bfloat16), cache_v, preferred_element_type=jnp.float32)
    m_ref[...] = jnp.broadcast_to(row_top, m_ref.shape)
    l_ref[...] = jnp.broadcast_to(row_total, l_ref.shape)


def cache_kernel(cvalid_ref, q_ref, acc_ref, m_ref, l_ref, *rest):
    cache_refs = rest[:-1]
    o_ref = rest[-1]
    cap_rows = cache_refs[0].shape[0] // 2
    tile_len = cache_refs[0].shape[1]
    score_scale = HS ** (-0.5)
    dims = (((1,), (1,)), ((), ()))
    head_q = q_ref[...]
    cache_k = jnp.concatenate(
        [ref[:cap_rows].reshape(cap_rows * tile_len, HS) for ref in cache_refs], axis=0
    )
    cache_v = jnp.concatenate(
        [ref[cap_rows:].reshape(cap_rows * tile_len, HS) for ref in cache_refs], axis=0
    )
    cache_scores = (
        lax.dot_general(head_q, cache_k, dims, preferred_element_type=jnp.float32) * score_scale
    )
    cache_scores = jnp.where(cvalid_ref[...] > 0, cache_scores, MASKED)
    first_top = m_ref[:, :1]
    row_top = jnp.maximum(first_top, jnp.max(cache_scores, axis=1, keepdims=True))
    rescale = jnp.exp(first_top - row_top)
    cache_exp = jnp.exp(cache_scores - row_top)
    row_total = l_ref[:, :1] * rescale + jnp.sum(cache_exp, axis=1, keepdims=True)
    mixed_out = acc_ref[...] * rescale + jnp.dot(
        cache_exp.astype(jnp.bfloat16), cache_v, preferred_element_type=jnp.float32
    )
    o_ref[...] = (mixed_out * (1.0 / row_total)).astype(jnp.bfloat16)


def pick_kernel(idx_ref, k_ref, v_ref, *o_refs):
    cap = o_refs[0].shape[0] // 2
    for d, o_ref in enumerate(o_refs):
        for c in range(cap):
            o_ref[c] = k_ref[idx_ref[cap * d + c]]
            o_ref[cap + c] = v_ref[idx_ref[cap * d + c]]


def body(
    query, keys, values, cache_keys, cache_values, q_gain, k_gain, window_margins, cache_frames
):
    frames_now = query.shape[1]
    tile_len = query.shape[2]
    channels = query.shape[3]
    width_all = channels * lax.axis_size("hd")
    own_place = lax.axis_index("sp")
    tile_count = lax.axis_size("sp")
    grid_rows = tile_count // GW
    own_cache_k = cache_keys[0]
    own_cache_v = cache_values[0]
    cap = cache_frames.shape[2]

    slot_ids = jnp.arange(9, dtype=jnp.int32)
    targets = jnp.clip(
        own_place - ((slot_ids // 3 - 1) * GW + (slot_ids % 3 - 1)), 0, tile_count - 1
    )
    listed = cache_frames[targets, slot_ids]
    wanted = jnp.clip(listed, 0, own_cache_k.shape[0] - 1).reshape(-1).astype(jnp.int32)
    full_spec = pl.BlockSpec(own_cache_k.shape, lambda i, idx: (0, 0, 0))
    out_block = (2 * cap,) + own_cache_k.shape[1:]
    picked = pl.pallas_call(
        pick_kernel,
        grid_spec=pltpu.PrefetchScalarGridSpec(
            num_scalar_prefetch=1,
            grid=(1,),
            in_specs=[full_spec, full_spec],
            out_specs=[pl.BlockSpec(out_block, lambda i, idx: (0, 0, 0)) for _ in range(9)],
        ),
        out_shape=[jax.ShapeDtypeStruct(out_block, own_cache_k.dtype) for _ in range(9)],
    )(wanted, own_cache_k, own_cache_v)

    cache_in = {}
    for row_step, col_step in STEPS:
        slot = slot_of(row_step, col_step)
        if (row_step, col_step) != (0, 0):
            shift_by = -(row_step * GW + col_step)
            cache_in[row_step, col_step] = shifted(picked[slot], "sp", shift_by)
        else:
            cache_in[row_step, col_step] = picked[slot]

    query_wide = query[0].astype(jnp.float32)
    keys_wide = keys[0].astype(jnp.float32)
    query_total, keys_total = hd_sum(
        jnp.stack(
            [jnp.sum(query_wide * query_wide, axis=-1), jnp.sum(keys_wide * keys_wide, axis=-1)]
        )
    )
    query_normed = normalize(query[0], q_gain, query_total, width_all)
    keys_normed = normalize(keys[0], k_gain, keys_total, width_all)
    key_grid = keys_normed.reshape(frames_now, TH, TW, channels)
    value_grid = values[0].reshape(frames_now, TH, TW, channels)
    both_grid = jnp.stack([key_grid, value_grid])

    edge_in = {}
    for row_step, col_step in STEPS:
        if (row_step, col_step) != (0, 0):
            shift_by = -(row_step * GW + col_step)
            edge_in[row_step, col_step] = shifted(
                edge_part(both_grid, row_step, col_step), "sp", shift_by
            )
    edge_in[0, 0] = both_grid
    bands = []
    for row_step in (-1, 0, 1):
        bands.append(
            jnp.concatenate([edge_in[row_step, col_step] for col_step in (-1, 0, 1)], axis=3)
        )
    window = jnp.concatenate(bands, axis=2)
    flat_wk = window[0].reshape(-1, channels)
    flat_wv = window[1].reshape(-1, channels)
    flat_q = query_normed.reshape(-1, channels)
    margins = window_margins[0]
    tile_row = own_place // GW
    tile_col = own_place % GW
    row_pos = jnp.arange(TH + 2 * HALO, dtype=jnp.int32)
    row_global = tile_row * TH - HALO + row_pos
    row_valid = (
        (row_global >= 0)
        & (row_global < grid_rows * TH)
        & (row_pos >= HALO - margins[0])
        & (row_pos < HALO + TH + margins[1])
    )
    col_pos = jnp.arange(TW + 2 * HALO, dtype=jnp.int32)
    col_global = tile_col * TW - HALO + col_pos
    col_valid = (
        (col_global >= 0)
        & (col_global < GW * TW)
        & (col_pos >= HALO - margins[2])
        & (col_pos < HALO + TW + margins[3])
    )
    window_valid = jnp.broadcast_to(
        (row_valid[:, None] & col_valid[None, :])[None], (frames_now, TH + 2 * HALO, TW + 2 * HALO)
    ).reshape(-1)
    own_listed = lax.dynamic_index_in_dim(cache_frames, own_place, 0, keepdims=False)
    cache_valid = jnp.broadcast_to(
        (own_listed >= 0)[:, :, None], (9, own_listed.shape[1], tile_len)
    ).reshape(-1)

    head_count = channels // HS
    query_rows = flat_q.shape[0]
    window_len = flat_wk.shape[0]
    block_len = 2 * cap * tile_len // 2
    cache_valid = cache_valid.astype(jnp.int32).reshape(9, block_len)
    center_valid = cache_valid[4][None, :]
    remote_valid = jnp.concatenate([cache_valid[:4], cache_valid[5:]], axis=0).reshape(1, -1)
    remote_list = [cache_in[step] for step in STEPS if step != (0, 0)]
    cache_spec = pl.BlockSpec((2 * cap, tile_len, HS), lambda h: (0, 0, h))
    head_spec = pl.BlockSpec((query_rows, HS), lambda h: (0, h))
    wide_shape = jax.ShapeDtypeStruct((query_rows, channels), jnp.float32)
    params = pltpu.CompilerParams(vmem_limit_bytes=60 * 1024 * 1024)
    first_acc, first_top, first_total = pl.pallas_call(
        window_kernel,
        grid=(head_count,),
        in_specs=[
            pl.BlockSpec((1, window_len), lambda h: (0, 0)),
            pl.BlockSpec((1, block_len), lambda h: (0, 0)),
            head_spec,
            pl.BlockSpec((window_len, HS), lambda h: (0, h)),
            pl.BlockSpec((window_len, HS), lambda h: (0, h)),
            cache_spec,
        ],
        out_specs=[head_spec, head_spec, head_spec],
        out_shape=[wide_shape, wide_shape, wide_shape],
        compiler_params=params,
    )(
        window_valid.astype(jnp.int32)[None, :],
        center_valid,
        flat_q,
        flat_wk,
        flat_wv,
        cache_in[0, 0],
    )
    heads_out = pl.pallas_call(
        cache_kernel,
        grid=(head_count,),
        in_specs=[
            pl.BlockSpec((1, remote_valid.shape[1]), lambda h: (0, 0)),
            head_spec,
            head_spec,
            head_spec,
            head_spec,
        ]
        + [cache_spec for _ in remote_list],
        out_specs=head_spec,
        out_shape=jax.ShapeDtypeStruct((query_rows, channels), jnp.bfloat16),
        compiler_params=params,
    )(remote_valid, flat_q, first_acc, first_top, first_total, *remote_list)
    result = heads_out.reshape(1, frames_now, tile_len, channels)
    return result


def solution(mesh):
    return jax.shard_map(
        body,
        mesh=mesh,
        in_specs=(
            P("sp", None, None, "hd"),
            P("sp", None, None, "hd"),
            P("sp", None, None, "hd"),
            P("sp", None, None, "hd"),
            P("sp", None, None, "hd"),
            P("hd"),
            P("hd"),
            P("sp", None),
            P(),
        ),
        out_specs=P("sp", None, None, "hd"),
        check_vma=False,
    )
```

```python
import jax
import jax.numpy as jnp
from jax import lax
from jax.sharding import PartitionSpec as P
from jax.experimental import pallas as pl
from jax.experimental.pallas import tpu as pltpu

HS = 128
TH = 8
TW = 16
GW = 8
HALO = 4


EPSILON = 1e-06
MASKED = -1e30
STEPS = [(r, c) for r in (-1, 0, 1) for c in (-1, 0, 1)]


def shifted(x, axis, by):
    size = lax.axis_size(axis)
    pairs = [(i, i + by) for i in range(size) if 0 <= i + by < size]
    return lax.ppermute(x, axis, pairs)


def edge_part(grid, row_step, col_step):
    if row_step == -1:
        grid = grid[:, :, TH - HALO :]
    elif row_step == 1:
        grid = grid[:, :, :HALO]
    if col_step == -1:
        grid = grid[:, :, :, TW - HALO :]
    elif col_step == 1:
        grid = grid[:, :, :, :HALO]
    return grid


def hd_sum(x):
    size = lax.axis_size("hd")
    step = 1
    while step < size:
        pairs = [(i, i ^ step) for i in range(size)]
        x = x + lax.ppermute(x, "hd", pairs)
        step *= 2
    return x


def slot_of(row_step, col_step):
    return 3 * (row_step + 1) + (col_step + 1)


def normalize(tensor, gain, row_total, width_all):
    wide = tensor.astype(jnp.float32)
    factor = lax.rsqrt(row_total / width_all + EPSILON)
    return (wide * factor[..., None] * gain).astype(jnp.bfloat16)


def window_kernel(wvalid_ref, cvalid_ref, q_ref, wk_ref, wv_ref, c_ref, acc_ref, m_ref, l_ref):
    cap_rows = c_ref.shape[0] // 2
    tile_len = c_ref.shape[1]
    score_scale = HS ** (-0.5)
    dims = (((1,), (1,)), ((), ()))
    head_q = q_ref[...]
    cache_k = c_ref[:cap_rows].reshape(cap_rows * tile_len, HS)
    cache_v = c_ref[cap_rows:].reshape(cap_rows * tile_len, HS)
    window_scores = (
        lax.dot_general(head_q, wk_ref[...], dims, preferred_element_type=jnp.float32)
        * score_scale
    )
    window_scores = jnp.where(wvalid_ref[...] > 0, window_scores, MASKED)
    cache_scores = (
        lax.dot_general(head_q, cache_k, dims, preferred_element_type=jnp.float32) * score_scale
    )
    cache_scores = jnp.where(cvalid_ref[...] > 0, cache_scores, MASKED)
    row_top = jnp.maximum(
        jnp.max(window_scores, axis=1, keepdims=True), jnp.max(cache_scores, axis=1, keepdims=True)
    )
    window_exp = jnp.exp(window_scores - row_top)
    cache_exp = jnp.exp(cache_scores - row_top)
    row_total = jnp.sum(window_exp, axis=1, keepdims=True) + jnp.sum(
        cache_exp, axis=1, keepdims=True
    )
    acc_ref[...] = jnp.dot(
        window_exp.astype(jnp.bfloat16), wv_ref[...], preferred_element_type=jnp.float32
    ) + jnp.dot(cache_exp.astype(jnp.bfloat16), cache_v, preferred_element_type=jnp.float32)
    m_ref[...] = jnp.broadcast_to(row_top, m_ref.shape)
    l_ref[...] = jnp.broadcast_to(row_total, l_ref.shape)


def cache_kernel(cvalid_ref, q_ref, acc_ref, m_ref, l_ref, *rest):
    cache_refs = rest[:-1]
    o_ref = rest[-1]
    cap_rows = cache_refs[0].shape[0] // 2
    tile_len = cache_refs[0].shape[1]
    score_scale = HS ** (-0.5)
    dims = (((1,), (1,)), ((), ()))
    head_q = q_ref[...]
    cache_k = jnp.concatenate(
        [ref[:cap_rows].reshape(cap_rows * tile_len, HS) for ref in cache_refs], axis=0
    )
    cache_v = jnp.concatenate(
        [ref[cap_rows:].reshape(cap_rows * tile_len, HS) for ref in cache_refs], axis=0
    )
    cache_scores = (
        lax.dot_general(head_q, cache_k, dims, preferred_element_type=jnp.float32) * score_scale
    )
    cache_scores = jnp.where(cvalid_ref[...] > 0, cache_scores, MASKED)
    first_top = m_ref[:, :1]
    row_top = jnp.maximum(first_top, jnp.max(cache_scores, axis=1, keepdims=True))
    rescale = jnp.exp(first_top - row_top)
    cache_exp = jnp.exp(cache_scores - row_top)
    row_total = l_ref[:, :1] * rescale + jnp.sum(cache_exp, axis=1, keepdims=True)
    mixed_out = acc_ref[...] * rescale + jnp.dot(
        cache_exp.astype(jnp.bfloat16), cache_v, preferred_element_type=jnp.float32
    )
    o_ref[...] = (mixed_out * (1.0 / row_total)).astype(jnp.bfloat16)


def pick_kernel(idx_ref, k_ref, v_ref, *o_refs):
    cap = o_refs[0].shape[0] // 2
    for d, o_ref in enumerate(o_refs):
        for c in range(cap):
            o_ref[c] = k_ref[idx_ref[cap * d + c]]
            o_ref[cap + c] = v_ref[idx_ref[cap * d + c]]


def body(
    query, keys, values, cache_keys, cache_values, q_gain, k_gain, window_margins, cache_frames
):
    frames_now = query.shape[1]
    tile_len = query.shape[2]
    channels = query.shape[3]
    width_all = channels * lax.axis_size("hd")
    own_place = lax.axis_index("sp")
    tile_count = lax.axis_size("sp")
    grid_rows = tile_count // GW
    own_cache_k = cache_keys[0]
    own_cache_v = cache_values[0]
    cap = cache_frames.shape[2]

    slot_ids = jnp.arange(9, dtype=jnp.int32)
    targets = jnp.clip(
        own_place - ((slot_ids // 3 - 1) * GW + (slot_ids % 3 - 1)), 0, tile_count - 1
    )
    listed = cache_frames[targets, slot_ids]
    wanted = jnp.clip(listed, 0, own_cache_k.shape[0] - 1).reshape(-1).astype(jnp.int32)
    full_spec = pl.BlockSpec(own_cache_k.shape, lambda i, idx: (0, 0, 0))
    out_block = (2 * cap,) + own_cache_k.shape[1:]
    picked = pl.pallas_call(
        pick_kernel,
        grid_spec=pltpu.PrefetchScalarGridSpec(
            num_scalar_prefetch=1,
            grid=(1,),
            in_specs=[full_spec, full_spec],
            out_specs=[pl.BlockSpec(out_block, lambda i, idx: (0, 0, 0)) for _ in range(9)],
        ),
        out_shape=[jax.ShapeDtypeStruct(out_block, own_cache_k.dtype) for _ in range(9)],
    )(wanted, own_cache_k, own_cache_v)

    cache_in = {}
    for row_step, col_step in STEPS:
        slot = slot_of(row_step, col_step)
        if (row_step, col_step) != (0, 0):
            shift_by = -(row_step * GW + col_step)
            cache_in[row_step, col_step] = shifted(picked[slot], "sp", shift_by)
        else:
            cache_in[row_step, col_step] = picked[slot]

    key_grid = keys[0].reshape(frames_now, TH, TW, channels)
    value_grid = values[0].reshape(frames_now, TH, TW, channels)
    both_grid = jnp.stack([key_grid, value_grid])

    edge_in = {}
    for row_step, col_step in STEPS:
        if (row_step, col_step) != (0, 0):
            shift_by = -(row_step * GW + col_step)
            edge_in[row_step, col_step] = shifted(
                edge_part(both_grid, row_step, col_step), "sp", shift_by
            )
    edge_in[0, 0] = both_grid
    bands = []
    for row_step in (-1, 0, 1):
        bands.append(
            jnp.concatenate([edge_in[row_step, col_step] for col_step in (-1, 0, 1)], axis=3)
        )
    window = jnp.concatenate(bands, axis=2)
    window_raw = window[0].reshape(-1, channels)
    query_wide = query[0].reshape(-1, channels).astype(jnp.float32)
    window_wide = window_raw.astype(jnp.float32)
    query_rows = query_wide.shape[0]
    row_sums = hd_sum(
        jnp.concatenate(
            [jnp.sum(query_wide * query_wide, axis=-1), jnp.sum(window_wide * window_wide, axis=-1)]
        )
    )
    query_normed = normalize(query[0].reshape(-1, channels), q_gain, row_sums[:query_rows], width_all)
    flat_wk = normalize(window_raw, k_gain, row_sums[query_rows:], width_all)
    flat_wv = window[1].reshape(-1, channels)
    flat_q = query_normed.reshape(-1, channels)
    margins = window_margins[0]
    tile_row = own_place // GW
    tile_col = own_place % GW
    row_pos = jnp.arange(TH + 2 * HALO, dtype=jnp.int32)
    row_global = tile_row * TH - HALO + row_pos
    row_valid = (
        (row_global >= 0)
        & (row_global < grid_rows * TH)
        & (row_pos >= HALO - margins[0])
        & (row_pos < HALO + TH + margins[1])
    )
    col_pos = jnp.arange(TW + 2 * HALO, dtype=jnp.int32)
    col_global = tile_col * TW - HALO + col_pos
    col_valid = (
        (col_global >= 0)
        & (col_global < GW * TW)
        & (col_pos >= HALO - margins[2])
        & (col_pos < HALO + TW + margins[3])
    )
    window_valid = jnp.broadcast_to(
        (row_valid[:, None] & col_valid[None, :])[None], (frames_now, TH + 2 * HALO, TW + 2 * HALO)
    ).reshape(-1)
    own_listed = lax.dynamic_index_in_dim(cache_frames, own_place, 0, keepdims=False)
    cache_valid = jnp.broadcast_to(
        (own_listed >= 0)[:, :, None], (9, own_listed.shape[1], tile_len)
    ).reshape(-1)

    head_count = channels // HS
    query_rows = flat_q.shape[0]
    window_len = flat_wk.shape[0]
    block_len = 2 * cap * tile_len // 2
    cache_valid = cache_valid.astype(jnp.int32).reshape(9, block_len)
    center_valid = cache_valid[4][None, :]
    remote_valid = jnp.concatenate([cache_valid[:4], cache_valid[5:]], axis=0).reshape(1, -1)
    remote_list = [cache_in[step] for step in STEPS if step != (0, 0)]
    cache_spec = pl.BlockSpec((2 * cap, tile_len, HS), lambda h: (0, 0, h))
    head_spec = pl.BlockSpec((query_rows, HS), lambda h: (0, h))
    wide_shape = jax.ShapeDtypeStruct((query_rows, channels), jnp.float32)
    params = pltpu.CompilerParams(vmem_limit_bytes=60 * 1024 * 1024)
    first_acc, first_top, first_total = pl.pallas_call(
        window_kernel,
        grid=(head_count,),
        in_specs=[
            pl.BlockSpec((1, window_len), lambda h: (0, 0)),
            pl.BlockSpec((1, block_len), lambda h: (0, 0)),
            head_spec,
            pl.BlockSpec((window_len, HS), lambda h: (0, h)),
            pl.BlockSpec((window_len, HS), lambda h: (0, h)),
            cache_spec,
        ],
        out_specs=[head_spec, head_spec, head_spec],
        out_shape=[wide_shape, wide_shape, wide_shape],
        compiler_params=params,
    )(
        window_valid.astype(jnp.int32)[None, :],
        center_valid,
        flat_q,
        flat_wk,
        flat_wv,
        cache_in[0, 0],
    )
    heads_out = pl.pallas_call(
        cache_kernel,
        grid=(head_count,),
        in_specs=[
            pl.BlockSpec((1, remote_valid.shape[1]), lambda h: (0, 0)),
            head_spec,
            head_spec,
            head_spec,
            head_spec,
        ]
        + [cache_spec for _ in remote_list],
        out_specs=head_spec,
        out_shape=jax.ShapeDtypeStruct((query_rows, channels), jnp.bfloat16),
        compiler_params=params,
    )(remote_valid, flat_q, first_acc, first_top, first_total, *remote_list)
    result = heads_out.reshape(1, frames_now, tile_len, channels)
    return result


def solution(mesh):
    return jax.shard_map(
        body,
        mesh=mesh,
        in_specs=(
            P("sp", None, None, "hd"),
            P("sp", None, None, "hd"),
            P("sp", None, None, "hd"),
            P("sp", None, None, "hd"),
            P("sp", None, None, "hd"),
            P("hd"),
            P("hd"),
            P("sp", None),
            P(),
        ),
        out_specs=P("sp", None, None, "hd"),
        check_vma=False,
    )
```

```python
import jax
import jax.numpy as jnp
from jax import lax
from jax.sharding import PartitionSpec as P
from jax.experimental import pallas as pl
from jax.experimental.pallas import tpu as pltpu

HS = 128
TH = 8
TW = 16
GW = 8
HALO = 4


EPSILON = 1e-06
MASKED = -1e30
STEPS = [(r, c) for r in (-1, 0, 1) for c in (-1, 0, 1)]


def shifted(x, axis, by):
    size = lax.axis_size(axis)
    pairs = [(i, i + by) for i in range(size) if 0 <= i + by < size]
    return lax.ppermute(x, axis, pairs)


def edge_part(grid, row_step, col_step):
    if row_step == -1:
        grid = grid[:, :, TH - HALO :]
    elif row_step == 1:
        grid = grid[:, :, :HALO]
    if col_step == -1:
        grid = grid[:, :, :, TW - HALO :]
    elif col_step == 1:
        grid = grid[:, :, :, :HALO]
    return grid


def hd_sum(x):
    size = lax.axis_size("hd")
    step = 1
    while step < size:
        pairs = [(i, i ^ step) for i in range(size)]
        x = x + lax.ppermute(x, "hd", pairs)
        step *= 2
    return x


def slot_of(row_step, col_step):
    return 3 * (row_step + 1) + (col_step + 1)


def normalize(tensor, gain, row_total, width_all):
    wide = tensor.astype(jnp.float32)
    factor = lax.rsqrt(row_total / width_all + EPSILON)
    return (wide * factor[..., None] * gain).astype(jnp.bfloat16)


def window_kernel(wvalid_ref, cvalid_ref, q_ref, wk_ref, wv_ref, c_ref, acc_ref, m_ref, l_ref):
    cap_rows = c_ref.shape[0] // 2
    tile_len = c_ref.shape[1]
    score_scale = HS ** (-0.5)
    dims = (((1,), (1,)), ((), ()))
    head_q = q_ref[...]
    cache_k = c_ref[:cap_rows].reshape(cap_rows * tile_len, HS)
    cache_v = c_ref[cap_rows:].reshape(cap_rows * tile_len, HS)
    window_scores = (
        lax.dot_general(head_q, wk_ref[...], dims, preferred_element_type=jnp.float32)
        * score_scale
    )
    window_scores = jnp.where(wvalid_ref[...] > 0, window_scores, MASKED)
    cache_scores = (
        lax.dot_general(head_q, cache_k, dims, preferred_element_type=jnp.float32) * score_scale
    )
    cache_scores = jnp.where(cvalid_ref[...] > 0, cache_scores, MASKED)
    row_top = jnp.maximum(
        jnp.max(window_scores, axis=1, keepdims=True), jnp.max(cache_scores, axis=1, keepdims=True)
    )
    window_exp = jnp.exp(window_scores - row_top)
    cache_exp = jnp.exp(cache_scores - row_top)
    row_total = jnp.sum(window_exp, axis=1, keepdims=True) + jnp.sum(
        cache_exp, axis=1, keepdims=True
    )
    acc_ref[...] = jnp.dot(
        window_exp.astype(jnp.bfloat16), wv_ref[...], preferred_element_type=jnp.float32
    ) + jnp.dot(cache_exp.astype(jnp.bfloat16), cache_v, preferred_element_type=jnp.float32)
    m_ref[...] = jnp.broadcast_to(row_top, m_ref.shape)
    l_ref[...] = jnp.broadcast_to(row_total, l_ref.shape)


def cache_kernel(cvalid_ref, q_ref, acc_ref, m_ref, l_ref, *rest):
    merge_step(cvalid_ref, q_ref, acc_ref, m_ref, l_ref, rest[:-1], rest[-1:])


def partial_kernel(cvalid_ref, q_ref, acc_ref, m_ref, l_ref, *rest):
    merge_step(cvalid_ref, q_ref, acc_ref, m_ref, l_ref, rest[:-3], rest[-3:])


def merge_step(cvalid_ref, q_ref, acc_ref, m_ref, l_ref, cache_refs, out_refs):
    cap_rows = cache_refs[0].shape[0] // 2
    tile_len = cache_refs[0].shape[1]
    score_scale = HS ** (-0.5)
    dims = (((1,), (1,)), ((), ()))
    head_q = q_ref[...]
    cache_k = jnp.concatenate(
        [ref[:cap_rows].reshape(cap_rows * tile_len, HS) for ref in cache_refs], axis=0
    )
    cache_v = jnp.concatenate(
        [ref[cap_rows:].reshape(cap_rows * tile_len, HS) for ref in cache_refs], axis=0
    )
    cache_scores = (
        lax.dot_general(head_q, cache_k, dims, preferred_element_type=jnp.float32) * score_scale
    )
    cache_scores = jnp.where(cvalid_ref[...] > 0, cache_scores, MASKED)
    first_top = m_ref[:, :1]
    row_top = jnp.maximum(first_top, jnp.max(cache_scores, axis=1, keepdims=True))
    rescale = jnp.exp(first_top - row_top)
    cache_exp = jnp.exp(cache_scores - row_top)
    row_total = l_ref[:, :1] * rescale + jnp.sum(cache_exp, axis=1, keepdims=True)
    mixed_out = acc_ref[...] * rescale + jnp.dot(
        cache_exp.astype(jnp.bfloat16), cache_v, preferred_element_type=jnp.float32
    )
    if len(out_refs) == 1:
        out_refs[0][...] = (mixed_out * (1.0 / row_total)).astype(jnp.bfloat16)
    else:
        out_refs[0][...] = mixed_out
        out_refs[1][...] = jnp.broadcast_to(row_top, out_refs[1].shape)
        out_refs[2][...] = jnp.broadcast_to(row_total, out_refs[2].shape)


def pick_kernel(idx_ref, k_ref, v_ref, *o_refs):
    cap = o_refs[0].shape[0] // 2
    for d, o_ref in enumerate(o_refs):
        for c in range(cap):
            o_ref[c] = k_ref[idx_ref[cap * d + c]]
            o_ref[cap + c] = v_ref[idx_ref[cap * d + c]]


def body(
    query, keys, values, cache_keys, cache_values, q_gain, k_gain, window_margins, cache_frames
):
    frames_now = query.shape[1]
    tile_len = query.shape[2]
    channels = query.shape[3]
    width_all = channels * lax.axis_size("hd")
    own_place = lax.axis_index("sp")
    tile_count = lax.axis_size("sp")
    grid_rows = tile_count // GW
    own_cache_k = cache_keys[0]
    own_cache_v = cache_values[0]
    cap = cache_frames.shape[2]

    slot_ids = jnp.arange(9, dtype=jnp.int32)
    targets = jnp.clip(
        own_place - ((slot_ids // 3 - 1) * GW + (slot_ids % 3 - 1)), 0, tile_count - 1
    )
    listed = cache_frames[targets, slot_ids]
    wanted = jnp.clip(listed, 0, own_cache_k.shape[0] - 1).reshape(-1).astype(jnp.int32)
    full_spec = pl.BlockSpec(own_cache_k.shape, lambda i, idx: (0, 0, 0))
    out_block = (2 * cap,) + own_cache_k.shape[1:]
    picked = pl.pallas_call(
        pick_kernel,
        grid_spec=pltpu.PrefetchScalarGridSpec(
            num_scalar_prefetch=1,
            grid=(1,),
            in_specs=[full_spec, full_spec],
            out_specs=[pl.BlockSpec(out_block, lambda i, idx: (0, 0, 0)) for _ in range(9)],
        ),
        out_shape=[jax.ShapeDtypeStruct(out_block, own_cache_k.dtype) for _ in range(9)],
    )(wanted, own_cache_k, own_cache_v)

    cache_in = {}
    for row_step, col_step in STEPS:
        slot = slot_of(row_step, col_step)
        if (row_step, col_step) != (0, 0):
            shift_by = -(row_step * GW + col_step)
            cache_in[row_step, col_step] = shifted(picked[slot], "sp", shift_by)
        else:
            cache_in[row_step, col_step] = picked[slot]

    query_wide = query[0].astype(jnp.float32)
    keys_wide = keys[0].astype(jnp.float32)
    query_total, keys_total = hd_sum(
        jnp.stack(
            [jnp.sum(query_wide * query_wide, axis=-1), jnp.sum(keys_wide * keys_wide, axis=-1)]
        )
    )
    query_normed = normalize(query[0], q_gain, query_total, width_all)
    keys_normed = normalize(keys[0], k_gain, keys_total, width_all)
    key_grid = keys_normed.reshape(frames_now, TH, TW, channels)
    value_grid = values[0].reshape(frames_now, TH, TW, channels)
    both_grid = jnp.stack([key_grid, value_grid])

    edge_in = {}
    for row_step, col_step in STEPS:
        if (row_step, col_step) != (0, 0):
            shift_by = -(row_step * GW + col_step)
            edge_in[row_step, col_step] = shifted(
                edge_part(both_grid, row_step, col_step), "sp", shift_by
            )
    edge_in[0, 0] = both_grid
    bands = []
    for row_step in (-1, 0, 1):
        bands.append(
            jnp.concatenate([edge_in[row_step, col_step] for col_step in (-1, 0, 1)], axis=3)
        )
    window = jnp.concatenate(bands, axis=2)
    flat_wk = window[0].reshape(-1, channels)
    flat_wv = window[1].reshape(-1, channels)
    flat_q = query_normed.reshape(-1, channels)
    margins = window_margins[0]
    tile_row = own_place // GW
    tile_col = own_place % GW
    row_pos = jnp.arange(TH + 2 * HALO, dtype=jnp.int32)
    row_global = tile_row * TH - HALO + row_pos
    row_valid = (
        (row_global >= 0)
        & (row_global < grid_rows * TH)
        & (row_pos >= HALO - margins[0])
        & (row_pos < HALO + TH + margins[1])
    )
    col_pos = jnp.arange(TW + 2 * HALO, dtype=jnp.int32)
    col_global = tile_col * TW - HALO + col_pos
    col_valid = (
        (col_global >= 0)
        & (col_global < GW * TW)
        & (col_pos >= HALO - margins[2])
        & (col_pos < HALO + TW + margins[3])
    )
    window_valid = jnp.broadcast_to(
        (row_valid[:, None] & col_valid[None, :])[None], (frames_now, TH + 2 * HALO, TW + 2 * HALO)
    ).reshape(-1)
    own_listed = lax.dynamic_index_in_dim(cache_frames, own_place, 0, keepdims=False)
    cache_valid = jnp.broadcast_to(
        (own_listed >= 0)[:, :, None], (9, own_listed.shape[1], tile_len)
    ).reshape(-1)

    head_count = channels // HS
    query_rows = flat_q.shape[0]
    window_len = flat_wk.shape[0]
    block_len = 2 * cap * tile_len // 2
    cache_valid = cache_valid.astype(jnp.int32).reshape(9, block_len)
    center_valid = cache_valid[4][None, :]
    remote_valid = jnp.concatenate([cache_valid[:4], cache_valid[5:]], axis=0).reshape(1, -1)
    remote_list = [cache_in[step] for step in STEPS if step != (0, 0)]
    cache_spec = pl.BlockSpec((2 * cap, tile_len, HS), lambda h: (0, 0, h))
    head_spec = pl.BlockSpec((query_rows, HS), lambda h: (0, h))
    wide_shape = jax.ShapeDtypeStruct((query_rows, channels), jnp.float32)
    params = pltpu.CompilerParams(vmem_limit_bytes=60 * 1024 * 1024)
    first_acc, first_top, first_total = pl.pallas_call(
        window_kernel,
        grid=(head_count,),
        in_specs=[
            pl.BlockSpec((1, window_len), lambda h: (0, 0)),
            pl.BlockSpec((1, block_len), lambda h: (0, 0)),
            head_spec,
            pl.BlockSpec((window_len, HS), lambda h: (0, h)),
            pl.BlockSpec((window_len, HS), lambda h: (0, h)),
            cache_spec,
        ],
        out_specs=[head_spec, head_spec, head_spec],
        out_shape=[wide_shape, wide_shape, wide_shape],
        compiler_params=params,
    )(
        window_valid.astype(jnp.int32)[None, :],
        center_valid,
        flat_q,
        flat_wk,
        flat_wv,
        cache_in[0, 0],
    )
    half = len(remote_list) // 2
    remote_valid = remote_valid.reshape(2, -1)

    def merge_call(kernel, valid, acc, top, total, blocks, out_specs, out_shape):
        return pl.pallas_call(
            kernel,
            grid=(head_count,),
            in_specs=[
                pl.BlockSpec((1, valid.shape[1]), lambda h: (0, 0)),
                head_spec,
                head_spec,
                head_spec,
                head_spec,
            ]
            + [cache_spec for _ in blocks],
            out_specs=out_specs,
            out_shape=out_shape,
            compiler_params=params,
        )(valid, flat_q, acc, top, total, *blocks)

    mid_acc, mid_top, mid_total = merge_call(
        partial_kernel,
        remote_valid[:1],
        first_acc,
        first_top,
        first_total,
        remote_list[:half],
        [head_spec, head_spec, head_spec],
        [wide_shape, wide_shape, wide_shape],
    )
    heads_out = merge_call(
        cache_kernel,
        remote_valid[1:],
        mid_acc,
        mid_top,
        mid_total,
        remote_list[half:],
        head_spec,
        jax.ShapeDtypeStruct((query_rows, channels), jnp.bfloat16),
    )
    result = heads_out.reshape(1, frames_now, tile_len, channels)
    return result


def solution(mesh):
    return jax.shard_map(
        body,
        mesh=mesh,
        in_specs=(
            P("sp", None, None, "hd"),
            P("sp", None, None, "hd"),
            P("sp", None, None, "hd"),
            P("sp", None, None, "hd"),
            P("sp", None, None, "hd"),
            P("hd"),
            P("hd"),
            P("sp", None),
            P(),
        ),
        out_specs=P("sp", None, None, "hd"),
        check_vma=False,
    )
```
